512 devices in a mesh: pipe: 32 (over z, x_hi), tensor: 16 (over x_lo, y, core).
Axes of the slice: x: 4 (x_hi: 2, x_lo: 2; x = x_hi * 2 + x_lo), y: 4, z: 16, core: 2. Of those that a mesh axis runs over, the one named last changes fastest.
Arguments:
- x_saved: bfloat16 [32, 2, 4096, 128], P('pipe', None, 'tensor'), may hold values from -6 to 6
- seed_grad: bfloat16 [32, 2, 4096, 128], P('pipe', None, 'tensor'), may hold values from -6 to 6
- gate_blocks: bfloat16 [32, 16, 7, 20, 4096], P('pipe', 'tensor'), may hold values from -0.1875 to 0.1875
- up_blocks: bfloat16 [32, 16, 7, 20, 4096], P('pipe', 'tensor'), may hold values from -0.1875 to 0.1875
- down_blocks: bfloat16 [32, 16, 7, 20, 4096], P('pipe', 'tensor'), may hold values from -0.1875 to 0.1875
- gate_rows: int32 [32, 16, 7, 20], P('pipe', 'tensor'), may hold values from -1 to 63, as said below
- down_rows: int32 [32, 16, 7, 20], P('pipe', 'tensor'), may hold values from -1 to 63, as said below
Outputs:
- grad_input: bfloat16 [32, 2, 4096, 128], P('pipe', None, 'tensor')
The draws below stay inside these ranges and needn't reach their ends.
Inputs may be any that keep to these rules, and one draw needn't show every extreme that they name: `gate_rows`: in one column of tiles the non-negative entries are distinct and come before the -1 entries. All columns of one tensor shard of one section hold the same number of kept tiles, from 12 to 20, and in every section one shard holds 20 in every column. `down_rows`: as for gate_rows, drawn independently.
All inputs are finite; a program needn't handle non-finite values.
Results may differ from the reference program's by a relative error of at most 0.007.
Values may be sent and summed in bfloat16 or wider, within the bound.
No kernel may reach another device: no remote copies, remote signals or barrier semaphores. Data moves between devices by JAX's collectives and lax.ppermute only.
A program may use at most 128 MiB of HBM per device.

```python
import jax
import jax.numpy as jnp
from jax import lax

D = 4096
BLK = 64
RCAP = 20
TOK = 128
MB = 2
RB = 64
COLS = 14
RLOW = 12
N_PIPE = 32
N_TENSOR = 16


def block_rows(key):
    sections = N_PIPE // 2
    slot_total = sections * N_TENSOR * COLS
    key_list = jax.random.split(key, slot_total + 2)
    orders = jax.vmap(lambda one_key: jax.random.permutation(one_key, RB))(key_list[:slot_total])[:, :RCAP]
    orders = orders.reshape(sections, N_TENSOR, COLS, RCAP)
    fill_counts = jax.random.randint(key_list[slot_total], (sections, N_TENSOR), RLOW, RCAP + 1)
    busiest = jax.random.randint(key_list[slot_total + 1], (sections,), 0, N_TENSOR)
    fill_counts = jnp.where(jnp.arange(N_TENSOR)[None, :] == busiest[:, None], RCAP, fill_counts)
    slot_index = jnp.arange(RCAP)
    row_table = jnp.where(slot_index[None, None, None, :] < fill_counts[:, :, None, None], orders, -1)
    row_table = row_table.reshape(sections, N_TENSOR, 2, COLS // 2, RCAP).transpose(0, 2, 1, 3, 4)
    return row_table.reshape(N_PIPE, N_TENSOR, COLS // 2, RCAP).astype(jnp.int32)


def draw_gate_rows(key, part):
    return block_rows(jax.random.fold_in(key, 11))


def draw_down_rows(key, part):
    return block_rows(jax.random.fold_in(key, 23))


def levels(rng, extent, shards, low, top_value):
    def one(axis_at, parts):
        heights = jax.random.uniform(jax.random.fold_in(jax.random.fold_in(rng, 6), axis_at), (parts,), jnp.float32, low / len(shards), top_value / len(shards))
        return jnp.repeat(jnp.exp(heights), extent[axis_at] // parts).reshape((-1,) + (1,) * (len(extent) - axis_at - 1))

    level = one(*shards[0])
    for cut in shards[1:]:
        level = level * one(*cut)
    return level


def noise(key, dims, deviation, bound, shards=(), kind=jnp.bfloat16):
    gain = levels(key, dims, shards, -0.22, 0.18) if shards else 1.0
    drawn = jax.random.normal(key, dims, jnp.float32) * deviation * gain
    return jnp.minimum(jnp.maximum(drawn, -bound), bound).astype(kind)


def setup_inputs(seed: int = 0) -> dict:
    arg_keys = jax.random.split(jax.random.key(seed), 8)
    x_saved = noise(arg_keys[0], (N_PIPE, MB, D, TOK), 1.0, 6.0, ((0, 32), (2, 16)))
    seed_grad = noise(arg_keys[1], (N_PIPE, MB, D, TOK), 1.0, 6.0, ((0, 32), (2, 16)))
    gate_blocks = noise(arg_keys[2], (N_PIPE, N_TENSOR, COLS // 2, RCAP, BLK * BLK), (D // 4) ** -0.5, 0.1875, ((0, 32), (1, 16)))
    up_blocks = noise(arg_keys[3], (N_PIPE, N_TENSOR, COLS // 2, RCAP, BLK * BLK), (D // 4) ** -0.5, 0.1875, ((0, 32), (1, 16)))
    down_blocks = noise(arg_keys[4], (N_PIPE, N_TENSOR, COLS // 2, RCAP, BLK * BLK), (D // 4) ** -0.5, 0.1875, ((0, 32), (1, 16)))
    gate_rows = draw_gate_rows(jax.random.fold_in(arg_keys[7], 71), 0)
    down_rows = draw_down_rows(jax.random.fold_in(arg_keys[7], 71), 0)
    return {"x_saved": x_saved, "seed_grad": seed_grad, "gate_blocks": gate_blocks, "up_blocks": up_blocks, "down_blocks": down_blocks, "gate_rows": gate_rows, "down_rows": down_rows}


def column_products(tile_set, row_ids, source, pattern):
    columns, slot_depth = row_ids.shape
    filled = (row_ids >= 0).reshape(-1)
    picked = jnp.take(source, jnp.maximum(row_ids, 0).reshape(-1).astype(jnp.int32), axis=0)
    picked = jnp.where(filled[:, None, None], picked, jnp.zeros_like(picked))
    picked = picked.reshape(columns, slot_depth, BLK, source.shape[2])
    tile_grid = tile_set.reshape(columns, slot_depth, BLK, BLK)
    return jnp.einsum(pattern, tile_grid.astype(jnp.float32), picked.astype(jnp.float32))

def layer_branch(x_full, cot_full, gate_set, up_set, down_set, gate_ids, down_ids):
    tokens_now = x_full.shape[1]
    columns, slot_depth = gate_ids.shape
    x_blocks = x_full.reshape(RB, BLK, tokens_now)
    cot_blocks = cot_full.reshape(RB, BLK, tokens_now)
    gate_value = column_products(gate_set, gate_ids, x_blocks, 'crkj,crkt->cjt')
    up_value = column_products(up_set, gate_ids, x_blocks, 'crkj,crkt->cjt')
    d_hidden = column_products(down_set, down_ids, cot_blocks, 'crjk,crkt->cjt')
    sigmoid_gate = jax.nn.sigmoid(gate_value)
    d_gate = (d_hidden * up_value * sigmoid_gate * (1.0 + gate_value * (1.0 - sigmoid_gate))).astype(jnp.bfloat16)
    d_up = (d_hidden * gate_value * sigmoid_gate).astype(jnp.bfloat16)
    gate_grid = gate_set.reshape(columns, slot_depth, BLK, BLK).astype(jnp.float32)
    up_grid = up_set.reshape(columns, slot_depth, BLK, BLK).astype(jnp.float32)
    per_slot = jnp.einsum('crkj,cjt->crkt', gate_grid, d_gate.astype(jnp.float32))
    per_slot = per_slot + jnp.einsum('crkj,cjt->crkt', up_grid, d_up.astype(jnp.float32))
    segment_ids = jnp.where(gate_ids >= 0, gate_ids, RB).reshape(-1).astype(jnp.int32)
    summed = jax.ops.segment_sum(per_slot.reshape(columns * slot_depth, BLK, tokens_now), segment_ids, num_segments=RB + 1)
    return summed[:RB].reshape(RB * BLK, tokens_now)

def section_tiles(blocks, device):
    first_device = (2 * (device // 2)).astype(jnp.int32)
    pair_blocks = lax.dynamic_slice_in_dim(blocks, first_device, 2, 0)
    return jnp.concatenate([pair_blocks[0], pair_blocks[1]], axis=1)

def reference(x_saved, seed_grad, gate_blocks, up_blocks, down_blocks, gate_rows, down_rows):
    sections = N_PIPE // 2
    device_ids = jnp.arange(N_PIPE, dtype=jnp.int32)
    last_section = device_ids // 2 == sections - 1

    def device_grad(device_items):
        device, x_full, cot_full = device_items
        gate_all = section_tiles(gate_blocks, device)
        up_all = section_tiles(up_blocks, device)
        down_all = section_tiles(down_blocks, device)
        gate_all_ids = section_tiles(gate_rows, device)
        down_all_ids = section_tiles(down_rows, device)

        def shard_term(branch_total, shard_index):
            term = layer_branch(x_full, cot_full, gate_all[shard_index], up_all[shard_index], down_all[shard_index], gate_all_ids[shard_index], down_all_ids[shard_index])
            return (branch_total + term, None)
        branch_total, unused = lax.scan(shard_term, jnp.zeros((D, TOK), jnp.float32), jnp.arange(N_TENSOR, dtype=jnp.int32))
        return (cot_full.astype(jnp.float32) + branch_total).astype(jnp.bfloat16)
    results = []
    previous = None
    for micro_step in range(MB):
        if micro_step == 0:
            cotangent = seed_grad[:, 0]
        else:
            from_next = jnp.concatenate([previous[2:], jnp.zeros_like(previous[:2])], axis=0)
            cotangent = jnp.where(last_section[:, None, None], seed_grad[:, micro_step], from_next)
        previous = lax.map(device_grad, (device_ids, x_saved[:, micro_step], cotangent))
        results.append(previous)
    return jnp.stack(results, axis=1)
```

```python
import jax
import jax.numpy as jnp
from jax import lax
from jax.sharding import PartitionSpec as P

BLK = 64
RS_BITS = (0, 3, 1, 2)


def flip_pairs(axis, bit):
    return [(i, i ^ (1 << bit)) for i in range(lax.axis_size(axis))]


def from_behind(block, axis, distance):
    devices = range(lax.axis_size(axis))
    route = [(i - distance, i) for i in devices if i - distance in devices]
    return lax.ppermute(block, axis, route)


def reduce_scatter_tensor(value):
    t = lax.axis_index("tensor")
    n_bits = lax.axis_size("tensor").bit_length() - 1
    rows = value.shape[0] >> n_bits
    cur = value.reshape((2,) * n_bits + (rows, value.shape[1]))
    held = list(range(n_bits - 1, -1, -1))
    for bit in RS_BITS:
        axis = held.index(bit)
        mine = (t >> bit) & 1
        keep = lax.dynamic_index_in_dim(cur, mine, axis, keepdims=False)
        send = lax.dynamic_index_in_dim(cur, 1 - mine, axis, keepdims=False)
        cur = keep + lax.ppermute(send, "tensor", flip_pairs("tensor", bit))
        held.pop(axis)
    return cur


def all_gather_tensor(panel):
    t = lax.axis_index("tensor")
    n_bits = lax.axis_size("tensor").bit_length() - 1
    lead = panel.shape[:-2]
    cur = panel
    held = []
    for bit in reversed(RS_BITS):
        mine = (t >> bit) & 1
        recv = lax.ppermute(cur, "tensor", flip_pairs("tensor", bit))
        lo = jnp.where(mine == 0, cur, recv)
        hi = jnp.where(mine == 0, recv, cur)
        cur = jnp.stack([lo, hi], axis=len(lead))
        held.insert(0, bit)
    order = sorted(range(n_bits), key=lambda i: -held[i])
    lead_n = len(lead)
    perm = list(range(lead_n)) + [lead_n + i for i in order] + [lead_n + n_bits, lead_n + n_bits + 1]
    cur = jnp.transpose(cur, perm)
    return cur.reshape(lead + (panel.shape[-2] << n_bits, panel.shape[-1]))


def dense_in(tiles, row_ids, pattern):
    columns, slot_depth = row_ids.shape
    row_blocks = 64
    onehot = (row_ids[:, :, None] == jnp.arange(row_blocks)[None, None, :]).astype(tiles.dtype)
    grid = tiles.reshape(columns, slot_depth, BLK, BLK)
    dense = jnp.einsum(pattern, onehot, grid, preferred_element_type=jnp.float32)
    return dense.astype(tiles.dtype).reshape(columns * BLK, row_blocks * BLK)


def half_weights(gate_blocks, up_blocks, down_blocks, gate_rows, down_rows):
    wg = dense_in(gate_blocks, gate_rows, "crq,crkj->cjqk")
    wu = dense_in(up_blocks, gate_rows, "crq,crkj->cjqk")
    wd = dense_in(down_blocks, down_rows, "crq,crjk->cjqk")
    return wg, wu, wd


def half_branch(weights, x_full, cot_full):
    wg, wu, wd = weights
    gate_value = jnp.dot(wg, x_full, preferred_element_type=jnp.float32)
    up_value = jnp.dot(wu, x_full, preferred_element_type=jnp.float32)
    d_hidden = jnp.dot(wd, cot_full, preferred_element_type=jnp.float32)
    sigmoid_gate = jax.nn.sigmoid(gate_value)
    d_gate = (
        d_hidden * up_value * sigmoid_gate * (1.0 + gate_value * (1.0 - sigmoid_gate))
    ).astype(jnp.bfloat16)
    d_up = (d_hidden * gate_value * sigmoid_gate).astype(jnp.bfloat16)
    contract = (((0,), (0,)), ((), ()))
    branch = lax.dot_general(wg, d_gate, contract, preferred_element_type=jnp.float32)
    return branch + lax.dot_general(wu, d_up, contract, preferred_element_type=jnp.float32)


def per_device(x_saved, seed_grad, gate_blocks, up_blocks, down_blocks, gate_rows, down_rows):
    pipe_index = lax.axis_index("pipe")
    last_section = pipe_index // 2 == lax.axis_size("pipe") // 2 - 1
    own = tuple(a[0, 0] for a in (gate_blocks, up_blocks, down_blocks, gate_rows, down_rows))
    theirs = lax.ppermute(own, "pipe", flip_pairs("pipe", 0))
    micro_total = x_saved.shape[1]

    first = jnp.stack([x_saved[0, 0], seed_grad[0, 0]])
    x0_full, cot0_full = all_gather_tensor(first)
    own_w = half_weights(*own)
    their_w = half_weights(*theirs)

    grads = []
    cot_full = cot0_full
    x_full = x0_full
    for micro_step in range(micro_total):
        if micro_step > 0:
            x_full = all_gather_tensor(x_saved[0, micro_step])
            arrived = from_behind(grads[-1], "pipe", -2)
            cot_panel = jnp.where(last_section, seed_grad[0, micro_step], arrived)
            cot_full = all_gather_tensor(cot_panel)
        else:
            cot_panel = seed_grad[0, 0]
        branch = half_branch(own_w, x_full, cot_full) + half_branch(their_w, x_full, cot_full)
        summed = reduce_scatter_tensor(branch)
        grads.append((cot_panel.astype(jnp.float32) + summed).astype(jnp.bfloat16))
    return jnp.stack(grads)[None]


def solution(mesh):
    return jax.shard_map(
        per_device,
        mesh=mesh,
        in_specs=(
            P("pipe", None, "tensor", None),
            P("pipe", None, "tensor", None),
            P("pipe", "tensor", None, None, None),
            P("pipe", "tensor", None, None, None),
            P("pipe", "tensor", None, None, None),
            P("pipe", "tensor", None, None),
            P("pipe", "tensor", None, None),
        ),
        out_specs=P("pipe", None, "tensor", None),
        check_vma=False,
    )
```

```python
import jax
import jax.numpy as jnp
from jax import lax
from jax.sharding import PartitionSpec as P

BLK = 64
RS_BITS = (0, 3, 1, 2)


def flip_pairs(axis, bit):
    return [(i, i ^ (1 << bit)) for i in range(lax.axis_size(axis))]


def from_behind(block, axis, distance):
    devices = range(lax.axis_size(axis))
    route = [(i - distance, i) for i in devices if i - distance in devices]
    return lax.ppermute(block, axis, route)


def reduce_scatter_tensor(value):
    t = lax.axis_index("tensor")
    n_bits = lax.axis_size("tensor").bit_length() - 1
    rows = value.shape[0] >> n_bits
    cur = value.reshape((2,) * n_bits + (rows, value.shape[1]))
    held = list(range(n_bits - 1, -1, -1))
    for bit in RS_BITS:
        axis = held.index(bit)
        mine = (t >> bit) & 1
        keep = lax.dynamic_index_in_dim(cur, mine, axis, keepdims=False)
        send = lax.dynamic_index_in_dim(cur, 1 - mine, axis, keepdims=False)
        cur = keep + lax.ppermute(send, "tensor", flip_pairs("tensor", bit))
        held.pop(axis)
    return cur


def all_gather_tensor(panel):
    t = lax.axis_index("tensor")
    n_bits = lax.axis_size("tensor").bit_length() - 1
    lead = panel.shape[:-2]
    cur = panel
    held = []
    for bit in reversed(RS_BITS):
        mine = (t >> bit) & 1
        recv = lax.ppermute(cur, "tensor", flip_pairs("tensor", bit))
        lo = jnp.where(mine == 0, cur, recv)
        hi = jnp.where(mine == 0, recv, cur)
        cur = jnp.stack([lo, hi], axis=len(lead))
        held.insert(0, bit)
    order = sorted(range(n_bits), key=lambda i: -held[i])
    lead_n = len(lead)
    perm = list(range(lead_n)) + [lead_n + i for i in order] + [lead_n + n_bits, lead_n + n_bits + 1]
    cur = jnp.transpose(cur, perm)
    return cur.reshape(lead + (panel.shape[-2] << n_bits, panel.shape[-1]))


def slot_onehot(row_ids, row_blocks):
    flat = row_ids.reshape(-1)
    return flat[:, None] == jnp.arange(row_blocks)[None, :]


def half_prep(gate_blocks, up_blocks, down_blocks, gate_rows, down_rows, row_blocks):
    columns, slot_depth = gate_rows.shape
    tile_shape = (columns, slot_depth, BLK, BLK)
    pick_g = slot_onehot(gate_rows, row_blocks)
    pick_d = slot_onehot(down_rows, row_blocks)
    return (
        gate_blocks.reshape(tile_shape),
        up_blocks.reshape(tile_shape),
        down_blocks.reshape(tile_shape),
        pick_g.astype(jnp.bfloat16),
        pick_d.astype(jnp.bfloat16),
        pick_g.T.astype(jnp.float32),
    )


def pick_tiles(pick, source, columns):
    row_blocks = pick.shape[1]
    tokens = source.shape[1]
    picked = jnp.dot(
        pick, source.reshape(row_blocks, BLK * tokens), preferred_element_type=jnp.float32
    ).astype(source.dtype)
    return picked.reshape(columns, -1, BLK, tokens)


def half_values(prep, x_full):
    gate_grid, up_grid, _, pick_g, _, _ = prep
    columns = gate_grid.shape[0]
    x_picked = pick_tiles(pick_g, x_full, columns)
    gate_value = jnp.einsum("crkj,crkt->cjt", gate_grid, x_picked, preferred_element_type=jnp.float32)
    up_value = jnp.einsum("crkj,crkt->cjt", up_grid, x_picked, preferred_element_type=jnp.float32)
    return gate_value, up_value


def half_branch(prep, values, cot_full):
    gate_grid, up_grid, down_grid, _, pick_d, scatter_g = prep
    gate_value, up_value = values
    columns, slot_depth = gate_grid.shape[:2]
    tokens = cot_full.shape[1]
    cot_picked = pick_tiles(pick_d, cot_full, columns)
    d_hidden = jnp.einsum("crjk,crkt->cjt", down_grid, cot_picked, preferred_element_type=jnp.float32)
    sigmoid_gate = jax.nn.sigmoid(gate_value)
    d_gate = (
        d_hidden * up_value * sigmoid_gate * (1.0 + gate_value * (1.0 - sigmoid_gate))
    ).astype(jnp.bfloat16)
    d_up = (d_hidden * gate_value * sigmoid_gate).astype(jnp.bfloat16)
    per_slot = jnp.einsum("crkj,cjt->crkt", gate_grid, d_gate, preferred_element_type=jnp.float32)
    per_slot = per_slot + jnp.einsum("crkj,cjt->crkt", up_grid, d_up, preferred_element_type=jnp.float32)
    summed = jnp.dot(
        scatter_g,
        per_slot.reshape(columns * slot_depth, BLK * tokens),
        precision=lax.Precision.HIGHEST,
        preferred_element_type=jnp.float32,
    )
    return summed.reshape(-1, tokens)


def per_device(x_saved, seed_grad, gate_blocks, up_blocks, down_blocks, gate_rows, down_rows):
    pipe_index = lax.axis_index("pipe")
    last_section = pipe_index // 2 == lax.axis_size("pipe") // 2 - 1
    own = tuple(a[0, 0] for a in (gate_blocks, up_blocks, down_blocks, gate_rows, down_rows))
    theirs = lax.ppermute(own, "pipe", flip_pairs("pipe", 0))
    micro_total = x_saved.shape[1]
    row_blocks = x_saved.shape[2] * lax.axis_size("tensor") // BLK

    first = jnp.stack([x_saved[0, 0], seed_grad[0, 0]] + [x_saved[0, k] for k in range(1, micro_total)])
    gathered = all_gather_tensor(first)
    x_fulls = [gathered[0]] + [gathered[1 + k] for k in range(1, micro_total)]
    own_prep = half_prep(*own, row_blocks)
    their_prep = half_prep(*theirs, row_blocks)

    grads = []
    cot_full = gathered[1]
    for micro_step in range(micro_total):
        x_full = x_fulls[micro_step]
        own_values = half_values(own_prep, x_full)
        their_values = half_values(their_prep, x_full)
        if micro_step > 0:
            arrived = from_behind(grads[-1], "pipe", -2)
            cot_panel = jnp.where(last_section, seed_grad[0, micro_step], arrived)
            cot_full = all_gather_tensor(cot_panel)
        else:
            cot_panel = seed_grad[0, 0]
        branch = half_branch(own_prep, own_values, cot_full)
        branch = branch + half_branch(their_prep, their_values, cot_full)
        summed = reduce_scatter_tensor(branch)
        grads.append((cot_panel.astype(jnp.float32) + summed).astype(jnp.bfloat16))
    return jnp.stack(grads)[None]


def solution(mesh):
    return jax.shard_map(
        per_device,
        mesh=mesh,
        in_specs=(
            P("pipe", None, "tensor", None),
            P("pipe", None, "tensor", None),
            P("pipe", "tensor", None, None, None),
            P("pipe", "tensor", None, None, None),
            P("pipe", "tensor", None, None, None),
            P("pipe", "tensor", None, None),
            P("pipe", "tensor", None, None),
        ),
        out_specs=P("pipe", None, "tensor", None),
        check_vma=False,
    )
```

```python
import jax
import jax.numpy as jnp
from jax import lax
from jax.sharding import PartitionSpec as P

BLK = 64
RS_BITS = (0, 3, 1, 2)


def flip_pairs(axis, bit):
    return [(i, i ^ (1 << bit)) for i in range(lax.axis_size(axis))]


def from_behind(block, axis, distance):
    devices = range(lax.axis_size(axis))
    route = [(i - distance, i) for i in devices if i - distance in devices]
    return lax.ppermute(block, axis, route)


def reduce_scatter_tensor(value):
    t = lax.axis_index("tensor")
    n_bits = lax.axis_size("tensor").bit_length() - 1
    rows = value.shape[0] >> n_bits
    cur = value.reshape((2,) * n_bits + (rows, value.shape[1]))
    held = list(range(n_bits - 1, -1, -1))
    for bit in RS_BITS:
        axis = held.index(bit)
        mine = (t >> bit) & 1
        keep = lax.dynamic_index_in_dim(cur, mine, axis, keepdims=False)
        send = lax.dynamic_index_in_dim(cur, 1 - mine, axis, keepdims=False)
        cur = keep + lax.ppermute(send, "tensor", flip_pairs("tensor", bit))
        held.pop(axis)
    return cur


def all_gather_tensor(panel):
    t = lax.axis_index("tensor")
    n_bits = lax.axis_size("tensor").bit_length() - 1
    lead = panel.shape[:-2]
    cur = panel
    held = []
    for bit in reversed(RS_BITS):
        mine = (t >> bit) & 1
        recv = lax.ppermute(cur, "tensor", flip_pairs("tensor", bit))
        lo = jnp.where(mine == 0, cur, recv)
        hi = jnp.where(mine == 0, recv, cur)
        cur = jnp.stack([lo, hi], axis=len(lead))
        held.insert(0, bit)
    order = sorted(range(n_bits), key=lambda i: -held[i])
    lead_n = len(lead)
    perm = list(range(lead_n)) + [lead_n + i for i in order] + [lead_n + n_bits, lead_n + n_bits + 1]
    cur = jnp.transpose(cur, perm)
    return cur.reshape(lead + (panel.shape[-2] << n_bits, panel.shape[-1]))


def half_weights(gate_blocks, up_blocks, down_blocks, gate_rows, down_rows, row_blocks):
    columns, slot_depth = gate_rows.shape
    tile_shape = (columns, slot_depth, BLK, BLK)
    paired = jnp.concatenate([gate_blocks.reshape(tile_shape), up_blocks.reshape(tile_shape)], axis=3)
    pick = (gate_rows[:, :, None] == jnp.arange(row_blocks)[None, None, :]).astype(paired.dtype)
    dense = jnp.einsum("crq,crkj->qkcj", pick, paired, preferred_element_type=jnp.float32)
    dense = dense.astype(paired.dtype).reshape(row_blocks * BLK, columns * 2 * BLK)
    pick_d = (down_rows.reshape(-1)[:, None] == jnp.arange(row_blocks)[None, :]).astype(paired.dtype)
    return dense, down_blocks.reshape(tile_shape), pick_d


FEATURES = (((0,), (0,)), ((), ()))
HIDDEN = (((1,), (1,)), ((), ()))


def half_values(weights, x_full):
    dense = weights[0]
    both = lax.dot_general(x_full, dense, FEATURES, preferred_element_type=jnp.float32)
    return both.reshape(both.shape[0], -1, 2 * BLK)


def half_branch(weights, both, cot_full):
    dense, down_grid, pick_d = weights
    columns = down_grid.shape[0]
    tokens = cot_full.shape[1]
    row_blocks = pick_d.shape[1]
    cot_picked = jnp.dot(
        pick_d, cot_full.reshape(row_blocks, BLK * tokens), preferred_element_type=jnp.float32
    ).astype(cot_full.dtype).reshape(columns, -1, BLK, tokens)
    d_hidden = jnp.einsum("crjk,crkt->tcj", down_grid, cot_picked, preferred_element_type=jnp.float32)
    gate_value = both[:, :, :BLK]
    up_value = both[:, :, BLK:]
    sigmoid_gate = jax.nn.sigmoid(gate_value)
    d_gate = (
        d_hidden * up_value * sigmoid_gate * (1.0 + gate_value * (1.0 - sigmoid_gate))
    ).astype(jnp.bfloat16)
    d_up = (d_hidden * gate_value * sigmoid_gate).astype(jnp.bfloat16)
    d_both = jnp.concatenate([d_gate, d_up], axis=2).reshape(tokens, -1)
    return lax.dot_general(dense, d_both, HIDDEN, preferred_element_type=jnp.float32)


def per_device(x_saved, seed_grad, gate_blocks, up_blocks, down_blocks, gate_rows, down_rows):
    pipe_index = lax.axis_index("pipe")
    last_section = pipe_index // 2 == lax.axis_size("pipe") // 2 - 1
    own = tuple(a[0, 0] for a in (gate_blocks, up_blocks, down_blocks, gate_rows, down_rows))
    theirs = lax.ppermute(own, "pipe", flip_pairs("pipe", 0))
    micro_total = x_saved.shape[1]
    row_blocks = x_saved.shape[2] * lax.axis_size("tensor") // BLK

    first = jnp.stack([x_saved[0, 0], seed_grad[0, 0]] + [x_saved[0, k] for k in range(1, micro_total)])
    gathered = all_gather_tensor(first)
    x_fulls = [gathered[0]] + [gathered[1 + k] for k in range(1, micro_total)]
    own_prep = half_weights(*own, row_blocks)
    their_prep = half_weights(*theirs, row_blocks)

    grads = []
    cot_full = gathered[1]
    for micro_step in range(micro_total):
        x_full = x_fulls[micro_step]
        own_values = half_values(own_prep, x_full)
        their_values = half_values(their_prep, x_full)
        if micro_step > 0:
            arrived = from_behind(grads[-1], "pipe", -2)
            cot_panel = jnp.where(last_section, seed_grad[0, micro_step], arrived)
            cot_full = all_gather_tensor(cot_panel)
        else:
            cot_panel = seed_grad[0, 0]
        branch = half_branch(own_prep, own_values, cot_full)
        branch = branch + half_branch(their_prep, their_values, cot_full)
        summed = reduce_scatter_tensor(branch)
        grads.append((cot_panel.astype(jnp.float32) + summed).astype(jnp.bfloat16))
    return jnp.stack(grads)[None]


def solution(mesh):
    return jax.shard_map(
        per_device,
        mesh=mesh,
        in_specs=(
            P("pipe", None, "tensor", None),
            P("pipe", None, "tensor", None),
            P("pipe", "tensor", None, None, None),
            P("pipe", "tensor", None, None, None),
            P("pipe", "tensor", None, None, None),
            P("pipe", "tensor", None, None),
            P("pipe", "tensor", None, None),
        ),
        out_specs=P("pipe", None, "tensor", None),
        check_vma=False,
    )
```

```python
import jax
import jax.numpy as jnp
from jax import lax
from jax.sharding import PartitionSpec as P

BLK = 64
RS_BITS = (0, 3, 1, 2)


def flip_pairs(axis, bit):
    return [(i, i ^ (1 << bit)) for i in range(lax.axis_size(axis))]


def from_behind(block, axis, distance):
    devices = range(lax.axis_size(axis))
    route = [(i - distance, i) for i in devices if i - distance in devices]
    return lax.ppermute(block, axis, route)


def reduce_scatter_tensor(value):
    t = lax.axis_index("tensor")
    n_bits = lax.axis_size("tensor").bit_length() - 1
    rows = value.shape[0] >> n_bits
    cur = value.reshape((2,) * n_bits + (rows, value.shape[1]))
    held = list(range(n_bits - 1, -1, -1))
    for bit in RS_BITS:
        axis = held.index(bit)
        mine = (t >> bit) & 1
        keep = lax.dynamic_index_in_dim(cur, mine, axis, keepdims=False)
        send = lax.dynamic_index_in_dim(cur, 1 - mine, axis, keepdims=False)
        cur = keep + lax.ppermute(send, "tensor", flip_pairs("tensor", bit))
        held.pop(axis)
    return cur


def all_gather_tensor(panel):
    t = lax.axis_index("tensor")
    n_bits = lax.axis_size("tensor").bit_length() - 1
    lead = panel.shape[:-2]
    cur = panel
    held = []
    for bit in reversed(RS_BITS):
        mine = (t >> bit) & 1
        recv = lax.ppermute(cur, "tensor", flip_pairs("tensor", bit))
        lo = jnp.where(mine == 0, cur, recv)
        hi = jnp.where(mine == 0, recv, cur)
        cur = jnp.stack([lo, hi], axis=len(lead))
        held.insert(0, bit)
    order = sorted(range(n_bits), key=lambda i: -held[i])
    lead_n = len(lead)
    perm = list(range(lead_n)) + [lead_n + i for i in order] + [lead_n + n_bits, lead_n + n_bits + 1]
    cur = jnp.transpose(cur, perm)
    return cur.reshape(lead + (panel.shape[-2] << n_bits, panel.shape[-1]))


def half_weights(gate_blocks, up_blocks, down_blocks, gate_rows, down_rows, row_blocks):
    columns, slot_depth = gate_rows.shape
    tile_shape = (columns, slot_depth, BLK, BLK)
    paired = jnp.concatenate([gate_blocks.reshape(tile_shape), up_blocks.reshape(tile_shape)], axis=3)
    pick = (gate_rows[:, :, None] == jnp.arange(row_blocks)[None, None, :]).astype(paired.dtype)
    dense = jnp.einsum("crq,crkj->qkcj", pick, paired, preferred_element_type=jnp.float32)
    dense = dense.astype(paired.dtype).reshape(row_blocks * BLK, columns * 2 * BLK)
    pick_d = (down_rows.reshape(-1)[:, None] == jnp.arange(row_blocks)[None, :]).astype(paired.dtype)
    return dense, down_blocks.reshape(tile_shape), pick_d


FEATURES = (((0,), (0,)), ((), ()))
HIDDEN = (((1,), (1,)), ((), ()))


def half_values(weights, x_full):
    dense = weights[0]
    both = lax.dot_general(x_full, dense, FEATURES, preferred_element_type=jnp.float32)
    return both.reshape(both.shape[0], -1, 2 * BLK)


def half_branch(weights, both, cot_full):
    dense, down_grid, pick_d = weights
    columns = down_grid.shape[0]
    tokens = cot_full.shape[1]
    row_blocks = pick_d.shape[1]
    cot_picked = jnp.dot(
        pick_d, cot_full.reshape(row_blocks, BLK * tokens), preferred_element_type=jnp.float32
    ).astype(cot_full.dtype).reshape(columns, -1, BLK, tokens)
    d_hidden = jnp.einsum("crjk,crkt->tcj", down_grid, cot_picked, preferred_element_type=jnp.float32)
    gate_value = both[:, :, :BLK]
    up_value = both[:, :, BLK:]
    sigmoid_gate = jax.nn.sigmoid(gate_value)
    d_gate = (
        d_hidden * up_value * sigmoid_gate * (1.0 + gate_value * (1.0 - sigmoid_gate))
    ).astype(jnp.bfloat16)
    d_up = (d_hidden * gate_value * sigmoid_gate).astype(jnp.bfloat16)
    d_both = jnp.concatenate([d_gate, d_up], axis=2).reshape(tokens, -1)
    return lax.dot_general(dense, d_both, HIDDEN, preferred_element_type=jnp.float32)


def per_device(x_saved, seed_grad, gate_blocks, up_blocks, down_blocks, gate_rows, down_rows):
    pipe_index = lax.axis_index("pipe")
    last_section = pipe_index // 2 == lax.axis_size("pipe") // 2 - 1
    own = tuple(a[0, 0] for a in (gate_blocks, up_blocks, down_blocks, gate_rows, down_rows))
    theirs = lax.ppermute(own, "pipe", flip_pairs("pipe", 0))
    micro_total = x_saved.shape[1]
    row_blocks = x_saved.shape[2] * lax.axis_size("tensor") // BLK

    first = jnp.stack([x_saved[0, 0], seed_grad[0, 0]] + [x_saved[0, k] for k in range(1, micro_total)])
    gathered = lax.all_gather(first, "tensor", axis=1, tiled=True)
    x_fulls = [gathered[0]] + [gathered[1 + k] for k in range(1, micro_total)]
    own_prep = half_weights(*own, row_blocks)
    their_prep = half_weights(*theirs, row_blocks)

    grads = []
    cot_full = gathered[1]
    for micro_step in range(micro_total):
        x_full = x_fulls[micro_step]
        own_values = half_values(own_prep, x_full)
        their_values = half_values(their_prep, x_full)
        if micro_step > 0:
            arrived = from_behind(grads[-1], "pipe", -2)
            cot_panel = jnp.where(last_section, seed_grad[0, micro_step], arrived)
            cot_full = all_gather_tensor(cot_panel)
        else:
            cot_panel = seed_grad[0, 0]
        branch = half_branch(own_prep, own_values, cot_full)
        branch = branch + half_branch(their_prep, their_values, cot_full)
        summed = reduce_scatter_tensor(branch)
        grads.append((cot_panel.astype(jnp.float32) + summed).astype(jnp.bfloat16))
    return jnp.stack(grads)[None]


def solution(mesh):
    return jax.shard_map(
        per_device,
        mesh=mesh,
        in_specs=(
            P("pipe", None, "tensor", None),
            P("pipe", None, "tensor", None),
            P("pipe", "tensor", None, None, None),
            P("pipe", "tensor", None, None, None),
            P("pipe", "tensor", None, None, None),
            P("pipe", "tensor", None, None),
            P("pipe", "tensor", None, None),
        ),
        out_specs=P("pipe", None, "tensor", None),
        check_vma=False,
    )
```

```python
import jax
import jax.numpy as jnp
from jax import lax
from jax.sharding import PartitionSpec as P

BLK = 64
RS_BITS = (0, 3, 1, 2)


def flip_pairs(axis, bit):
    return [(i, i ^ (1 << bit)) for i in range(lax.axis_size(axis))]


def from_behind(block, axis, distance):
    devices = range(lax.axis_size(axis))
    route = [(i - distance, i) for i in devices if i - distance in devices]
    return lax.ppermute(block, axis, route)


def reduce_scatter_tensor(value):
    t = lax.axis_index("tensor")
    n_bits = lax.axis_size("tensor").bit_length() - 1
    rows = value.shape[0] >> n_bits
    cur = value.reshape((2,) * n_bits + (rows, value.shape[1]))
    held = list(range(n_bits - 1, -1, -1))
    for bit in RS_BITS:
        axis = held.index(bit)
        mine = (t >> bit) & 1
        keep = lax.dynamic_index_in_dim(cur, mine, axis, keepdims=False)
        send = lax.dynamic_index_in_dim(cur, 1 - mine, axis, keepdims=False)
        cur = keep + lax.ppermute(send, "tensor", flip_pairs("tensor", bit))
        held.pop(axis)
    return cur


def gather_bits(cur, held, bits):
    t = lax.axis_index("tensor")
    held = list(held)
    for bit in bits:
        mine = (t >> bit) & 1
        recv = lax.ppermute(cur, "tensor", flip_pairs("tensor", bit))
        lo = jnp.where(mine == 0, cur, recv)
        hi = jnp.where(mine == 0, recv, cur)
        cur = jnp.stack([lo, hi], axis=0)
        held.insert(0, bit)
    order = sorted(range(len(held)), key=lambda i: -held[i])
    cur = jnp.transpose(cur, order + [len(held), len(held) + 1])
    rows = cur.shape[-2] << len(held)
    return cur.reshape(rows, cur.shape[-1])


def all_gather_tensor(panel):
    return gather_bits(panel, [], reversed(RS_BITS))


Y_FLIPS = (0, 2, 4, 6)


def send_back_spread(panel):
    n_pipe = lax.axis_size("pipe")
    n_tensor = lax.axis_size("tensor")
    recvs = []
    for flip in Y_FLIPS:
        route = [
            (src_p * n_tensor + src_t, (src_p - 2) * n_tensor + (src_t ^ flip))
            for src_p in range(2, n_pipe)
            for src_t in range(n_tensor)
        ]
        recvs.append(lax.ppermute(panel, ("pipe", "tensor"), route))
    t = lax.axis_index("tensor")
    blocks = jnp.stack(recvs).reshape((2, 2) + panel.shape)
    blocks = jnp.where(((t >> 2) & 1) == 1, blocks[::-1], blocks)
    blocks = jnp.where(((t >> 1) & 1) == 1, blocks[:, ::-1], blocks)
    return recvs[0], blocks


def half_weights(gate_blocks, up_blocks, down_blocks, gate_rows, down_rows, row_blocks):
    columns, slot_depth = gate_rows.shape
    tile_shape = (columns, slot_depth, BLK, BLK)
    paired = jnp.concatenate([gate_blocks.reshape(tile_shape), up_blocks.reshape(tile_shape)], axis=3)
    pick = (gate_rows[:, :, None] == jnp.arange(row_blocks)[None, None, :]).astype(paired.dtype)
    dense = jnp.einsum("crq,crkj->qkcj", pick, paired, preferred_element_type=jnp.float32)
    dense = dense.astype(paired.dtype).reshape(row_blocks * BLK, columns * 2 * BLK)
    pick_d = (down_rows.reshape(-1)[:, None] == jnp.arange(row_blocks)[None, :]).astype(paired.dtype)
    return dense, down_blocks.reshape(tile_shape), pick_d


FEATURES = (((0,), (0,)), ((), ()))
HIDDEN = (((1,), (1,)), ((), ()))


def half_values(weights, x_full):
    dense = weights[0]
    both = lax.dot_general(x_full, dense, FEATURES, preferred_element_type=jnp.float32)
    return both.reshape(both.shape[0], -1, 2 * BLK)


def half_branch(weights, both, cot_full):
    dense, down_grid, pick_d = weights
    columns = down_grid.shape[0]
    tokens = cot_full.shape[1]
    row_blocks = pick_d.shape[1]
    cot_picked = jnp.dot(
        pick_d, cot_full.reshape(row_blocks, BLK * tokens), preferred_element_type=jnp.float32
    ).astype(cot_full.dtype).reshape(columns, -1, BLK, tokens)
    d_hidden = jnp.einsum("crjk,crkt->tcj", down_grid, cot_picked, preferred_element_type=jnp.float32)
    gate_value = both[:, :, :BLK]
    up_value = both[:, :, BLK:]
    sigmoid_gate = jax.nn.sigmoid(gate_value)
    d_gate = (
        d_hidden * up_value * sigmoid_gate * (1.0 + gate_value * (1.0 - sigmoid_gate))
    ).astype(jnp.bfloat16)
    d_up = (d_hidden * gate_value * sigmoid_gate).astype(jnp.bfloat16)
    d_both = jnp.concatenate([d_gate, d_up], axis=2).reshape(tokens, -1)
    return lax.dot_general(dense, d_both, HIDDEN, preferred_element_type=jnp.float32)


def per_device(x_saved, seed_grad, gate_blocks, up_blocks, down_blocks, gate_rows, down_rows):
    pipe_index = lax.axis_index("pipe")
    last_section = pipe_index // 2 == lax.axis_size("pipe") // 2 - 1
    own = tuple(a[0, 0] for a in (gate_blocks, up_blocks, down_blocks, gate_rows, down_rows))
    theirs = lax.ppermute(own, "pipe", flip_pairs("pipe", 0))
    micro_total = x_saved.shape[1]
    row_blocks = x_saved.shape[2] * lax.axis_size("tensor") // BLK

    first = jnp.concatenate([x_saved[0], seed_grad[0]])
    gathered = lax.all_gather(first, "tensor", axis=1, tiled=True)
    x_fulls = [gathered[k] for k in range(micro_total)]
    own_prep = half_weights(*own, row_blocks)
    their_prep = half_weights(*theirs, row_blocks)

    grads = []
    cot_full = gathered[micro_total]
    for micro_step in range(micro_total):
        x_full = x_fulls[micro_step]
        own_values = half_values(own_prep, x_full)
        their_values = half_values(their_prep, x_full)
        if micro_step > 0:
            arrived, blocks = send_back_spread(grads[-1])
            cot_panel = jnp.where(last_section, seed_grad[0, micro_step], arrived)
            arrived_full = gather_bits(blocks, [2, 1], (3, 0))
            cot_full = jnp.where(last_section, gathered[micro_total + micro_step], arrived_full)
        else:
            cot_panel = seed_grad[0, 0]
        branch = half_branch(own_prep, own_values, cot_full)
        branch = branch + half_branch(their_prep, their_values, cot_full)
        summed = reduce_scatter_tensor(branch)
        grads.append((cot_panel.astype(jnp.float32) + summed).astype(jnp.bfloat16))
    return jnp.stack(grads)[None]


def solution(mesh):
    return jax.shard_map(
        per_device,
        mesh=mesh,
        in_specs=(
            P("pipe", None, "tensor", None),
            P("pipe", None, "tensor", None),
            P("pipe", "tensor", None, None, None),
            P("pipe", "tensor", None, None, None),
            P("pipe", "tensor", None, None, None),
            P("pipe", "tensor", None, None),
            P("pipe", "tensor", None, None),
        ),
        out_specs=P("pipe", None, "tensor", None),
        check_vma=False,
    )
```

```python
import jax
import jax.numpy as jnp
from jax import lax
from jax.sharding import PartitionSpec as P

BLK = 64
RS_BITS = (0, 3, 1, 2)


def flip_pairs(axis, bit):
    return [(i, i ^ (1 << bit)) for i in range(lax.axis_size(axis))]


def from_behind(block, axis, distance):
    devices = range(lax.axis_size(axis))
    route = [(i - distance, i) for i in devices if i - distance in devices]
    return lax.ppermute(block, axis, route)


def reduce_scatter_tensor(value):
    t = lax.axis_index("tensor")
    n_bits = lax.axis_size("tensor").bit_length() - 1
    rows = value.shape[0] >> n_bits
    cur = value.reshape((2,) * n_bits + (rows, value.shape[1]))
    held = list(range(n_bits - 1, -1, -1))
    for bit in RS_BITS:
        axis = held.index(bit)
        mine = (t >> bit) & 1
        keep = lax.dynamic_index_in_dim(cur, mine, axis, keepdims=False)
        send = lax.dynamic_index_in_dim(cur, 1 - mine, axis, keepdims=False)
        cur = keep + lax.ppermute(send, "tensor", flip_pairs("tensor", bit))
        held.pop(axis)
    return cur


def gather_bits(cur, held, bits):
    t = lax.axis_index("tensor")
    held = list(held)
    for bit in bits:
        mine = (t >> bit) & 1
        recv = lax.ppermute(cur, "tensor", flip_pairs("tensor", bit))
        lo = jnp.where(mine == 0, cur, recv)
        hi = jnp.where(mine == 0, recv, cur)
        cur = jnp.stack([lo, hi], axis=0)
        held.insert(0, bit)
    order = sorted(range(len(held)), key=lambda i: -held[i])
    cur = jnp.transpose(cur, order + [len(held), len(held) + 1])
    rows = cur.shape[-2] << len(held)
    return cur.reshape(rows, cur.shape[-1])


def all_gather_tensor(panel):
    return gather_bits(panel, [], reversed(RS_BITS))


Y_FLIPS = (0, 2, 4, 6)


def send_back_spread(panel):
    n_pipe = lax.axis_size("pipe")
    n_tensor = lax.axis_size("tensor")
    recvs = []
    for flip in Y_FLIPS:
        route = [
            (src_p * n_tensor + src_t, (src_p - 2) * n_tensor + (src_t ^ flip))
            for src_p in range(2, n_pipe)
            for src_t in range(n_tensor)
        ]
        recvs.append(lax.ppermute(panel, ("pipe", "tensor"), route))
    t = lax.axis_index("tensor")
    blocks = jnp.stack(recvs).reshape((2, 2) + panel.shape)
    blocks = jnp.where(((t >> 2) & 1) == 1, blocks[::-1], blocks)
    blocks = jnp.where(((t >> 1) & 1) == 1, blocks[:, ::-1], blocks)
    return recvs[0], blocks


def half_weights(gate_blocks, up_blocks, down_blocks, gate_rows, down_rows, row_blocks):
    columns, slot_depth = gate_rows.shape
    tile_shape = (columns, slot_depth, BLK, BLK)
    paired = jnp.concatenate([gate_blocks.reshape(tile_shape), up_blocks.reshape(tile_shape)], axis=3)
    pick = (gate_rows[:, :, None] == jnp.arange(row_blocks)[None, None, :]).astype(paired.dtype)
    dense = jnp.einsum("crq,crkj->qkcj", pick, paired, preferred_element_type=jnp.float32)
    dense = dense.astype(paired.dtype).reshape(row_blocks * BLK, columns * 2 * BLK)
    pick_d = (down_rows.reshape(-1)[:, None] == jnp.arange(row_blocks)[None, :]).astype(paired.dtype)
    return dense, down_blocks.reshape(tile_shape), pick_d


FEATURES = (((0,), (0,)), ((), ()))
HIDDEN = (((1,), (1,)), ((), ()))


def half_values(weights, x_all, micro_total):
    dense = weights[0]
    both = lax.dot_general(x_all, dense, FEATURES, preferred_element_type=jnp.float32)
    both = both.reshape(micro_total, -1, dense.shape[1] // (2 * BLK), 2 * BLK)
    return [both[k] for k in range(micro_total)]


def half_branch(weights, both, cot_full):
    dense, down_grid, pick_d = weights
    columns = down_grid.shape[0]
    tokens = cot_full.shape[1]
    row_blocks = pick_d.shape[1]
    cot_picked = jnp.dot(
        pick_d, cot_full.reshape(row_blocks, BLK * tokens), preferred_element_type=jnp.float32
    ).astype(cot_full.dtype).reshape(columns, -1, BLK, tokens)
    d_hidden = jnp.einsum("crjk,crkt->tcj", down_grid, cot_picked, preferred_element_type=jnp.float32)
    gate_value = both[:, :, :BLK]
    up_value = both[:, :, BLK:]
    sigmoid_gate = jax.nn.sigmoid(gate_value)
    d_gate = (
        d_hidden * up_value * sigmoid_gate * (1.0 + gate_value * (1.0 - sigmoid_gate))
    ).astype(jnp.bfloat16)
    d_up = (d_hidden * gate_value * sigmoid_gate).astype(jnp.bfloat16)
    d_both = jnp.concatenate([d_gate, d_up], axis=2).reshape(tokens, -1)
    return lax.dot_general(dense, d_both, HIDDEN, preferred_element_type=jnp.float32)


def per_device(x_saved, seed_grad, gate_blocks, up_blocks, down_blocks, gate_rows, down_rows):
    pipe_index = lax.axis_index("pipe")
    last_section = pipe_index // 2 == lax.axis_size("pipe") // 2 - 1
    own = tuple(a[0, 0] for a in (gate_blocks, up_blocks, down_blocks, gate_rows, down_rows))
    theirs = lax.ppermute(own, "pipe", flip_pairs("pipe", 0))
    micro_total = x_saved.shape[1]
    row_blocks = x_saved.shape[2] * lax.axis_size("tensor") // BLK

    tokens = x_saved.shape[3]
    first = jnp.concatenate([x_saved[0, k] for k in range(micro_total)] + [seed_grad[0, k] for k in range(micro_total)], axis=1)
    gathered_all = lax.all_gather(first, "tensor", axis=0, tiled=True)
    x_all = gathered_all[:, : micro_total * tokens]
    gathered = [gathered_all[:, k * tokens : (k + 1) * tokens] for k in range(2 * micro_total)]
    own_prep = half_weights(*own, row_blocks)
    their_prep = half_weights(*theirs, row_blocks)

    grads = []
    cot_full = gathered[micro_total]
    own_all = half_values(own_prep, x_all, micro_total)
    their_all = half_values(their_prep, x_all, micro_total)
    for micro_step in range(micro_total):
        own_values = own_all[micro_step]
        their_values = their_all[micro_step]
        if micro_step > 0:
            arrived, blocks = send_back_spread(grads[-1])
            cot_panel = jnp.where(last_section, seed_grad[0, micro_step], arrived)
            arrived_full = gather_bits(blocks, [2, 1], (3, 0))
            cot_full = jnp.where(last_section, gathered[micro_total + micro_step], arrived_full)
        else:
            cot_panel = seed_grad[0, 0]
        branch = half_branch(own_prep, own_values, cot_full)
        branch = branch + half_branch(their_prep, their_values, cot_full)
        summed = reduce_scatter_tensor(branch)
        grads.append((cot_panel.astype(jnp.float32) + summed).astype(jnp.bfloat16))
    return jnp.stack(grads)[None]


def solution(mesh):
    return jax.shard_map(
        per_device,
        mesh=mesh,
        in_specs=(
            P("pipe", None, "tensor", None),
            P("pipe", None, "tensor", None),
            P("pipe", "tensor", None, None, None),
            P("pipe", "tensor", None, None, None),
            P("pipe", "tensor", None, None, None),
            P("pipe", "tensor", None, None),
            P("pipe", "tensor", None, None),
        ),
        out_specs=P("pipe", None, "tensor", None),
        check_vma=False,
    )
```

```python
import jax
import jax.numpy as jnp
from jax import lax
from jax.sharding import PartitionSpec as P

BLK = 64
RS_BITS = (0, 3, 1, 2)


def flip_pairs(axis, bit):
    return [(i, i ^ (1 << bit)) for i in range(lax.axis_size(axis))]


def from_behind(block, axis, distance):
    devices = range(lax.axis_size(axis))
    route = [(i - distance, i) for i in devices if i - distance in devices]
    return lax.ppermute(block, axis, route)


def reduce_scatter_tensor(value):
    t = lax.axis_index("tensor")
    n_bits = lax.axis_size("tensor").bit_length() - 1
    rows = value.shape[0] >> n_bits
    cur = value.reshape((2,) * n_bits + (rows, value.shape[1]))
    held = list(range(n_bits - 1, -1, -1))
    for bit in RS_BITS:
        axis = held.index(bit)
        mine = (t >> bit) & 1
        keep = lax.dynamic_index_in_dim(cur, mine, axis, keepdims=False)
        send = lax.dynamic_index_in_dim(cur, 1 - mine, axis, keepdims=False)
        cur = keep + lax.ppermute(send, "tensor", flip_pairs("tensor", bit))
        held.pop(axis)
    return cur


def gather_bits(cur, held, bits):
    t = lax.axis_index("tensor")
    held = list(held)
    for bit in bits:
        mine = (t >> bit) & 1
        recv = lax.ppermute(cur, "tensor", flip_pairs("tensor", bit))
        lo = jnp.where(mine == 0, cur, recv)
        hi = jnp.where(mine == 0, recv, cur)
        cur = jnp.stack([lo, hi], axis=0)
        held.insert(0, bit)
    order = sorted(range(len(held)), key=lambda i: -held[i])
    cur = jnp.transpose(cur, order + [len(held), len(held) + 1])
    rows = cur.shape[-2] << len(held)
    return cur.reshape(rows, cur.shape[-1])


def all_gather_tensor(panel):
    return gather_bits(panel, [], reversed(RS_BITS))


Y_FLIPS = (0, 2, 4, 6)


def send_back_spread(panel):
    n_pipe = lax.axis_size("pipe")
    n_tensor = lax.axis_size("tensor")
    recvs = []
    for flip in Y_FLIPS:
        route = [
            (src_p * n_tensor + src_t, (src_p - 2) * n_tensor + (src_t ^ flip))
            for src_p in range(2, n_pipe)
            for src_t in range(n_tensor)
        ]
        recvs.append(lax.ppermute(panel, ("pipe", "tensor"), route))
    t = lax.axis_index("tensor")
    blocks = jnp.stack(recvs).reshape((2, 2) + panel.shape)
    blocks = jnp.where(((t >> 2) & 1) == 1, blocks[::-1], blocks)
    blocks = jnp.where(((t >> 1) & 1) == 1, blocks[:, ::-1], blocks)
    return recvs[0], blocks


def half_weights(gate_blocks, up_blocks, down_blocks, gate_rows, down_rows, row_blocks):
    columns, slot_depth = gate_rows.shape
    tile_shape = (columns, slot_depth, BLK, BLK)
    paired = jnp.concatenate([gate_blocks.reshape(tile_shape), up_blocks.reshape(tile_shape)], axis=3)
    pick = (gate_rows[:, :, None] == jnp.arange(row_blocks)[None, None, :]).astype(paired.dtype)
    dense = jnp.einsum("crq,crkj->qkcj", pick, paired, preferred_element_type=jnp.float32)
    dense = dense.astype(paired.dtype).reshape(row_blocks * BLK, columns * 2 * BLK)
    pick_d = (down_rows.reshape(-1)[:, None] == jnp.arange(row_blocks)[None, :]).astype(paired.dtype)
    return dense, down_blocks.reshape(tile_shape), pick_d


FEATURES = (((0,), (0,)), ((), ()))
HIDDEN = (((1,), (1,)), ((), ()))


def half_values(weights, x_all, micro_total):
    dense = weights[0]
    both = lax.dot_general(x_all, dense, FEATURES, preferred_element_type=jnp.float32)
    both = both.reshape(micro_total, -1, dense.shape[1] // (2 * BLK), 2 * BLK)
    return [both[k] for k in range(micro_total)]


def half_branch(weights, both, cot_full):
    dense, down_grid, pick_d = weights
    columns = down_grid.shape[0]
    tokens = cot_full.shape[1]
    row_blocks = pick_d.shape[1]
    cot_picked = jnp.dot(
        pick_d, cot_full.reshape(row_blocks, BLK * tokens), preferred_element_type=jnp.float32
    ).astype(cot_full.dtype).reshape(columns, -1, BLK, tokens)
    d_hidden = jnp.einsum("crjk,crkt->tcj", down_grid, cot_picked, preferred_element_type=jnp.float32)
    gate_value = both[:, :, :BLK]
    up_value = both[:, :, BLK:]
    sigmoid_gate = jax.nn.sigmoid(gate_value)
    d_gate = (
        d_hidden * up_value * sigmoid_gate * (1.0 + gate_value * (1.0 - sigmoid_gate))
    ).astype(jnp.bfloat16)
    d_up = (d_hidden * gate_value * sigmoid_gate).astype(jnp.bfloat16)
    d_both = jnp.concatenate([d_gate, d_up], axis=2).reshape(tokens, -1)
    return lax.dot_general(dense, d_both, HIDDEN, preferred_element_type=jnp.float32)


def per_device(x_saved, seed_grad, gate_blocks, up_blocks, down_blocks, gate_rows, down_rows):
    pipe_index = lax.axis_index("pipe")
    last_section = pipe_index // 2 == lax.axis_size("pipe") // 2 - 1
    own = tuple(a[0, 0] for a in (gate_blocks, up_blocks, down_blocks, gate_rows, down_rows))
    theirs = lax.ppermute(own, "pipe", flip_pairs("pipe", 0))
    micro_total = x_saved.shape[1]
    row_blocks = x_saved.shape[2] * lax.axis_size("tensor") // BLK

    tokens = x_saved.shape[3]
    first = jnp.concatenate([x_saved[0, k] for k in range(micro_total)] + [seed_grad[0, k] for k in range(micro_total)], axis=1)
    gathered_all = lax.all_gather(first, "tensor", axis=0, tiled=True)
    x_all = gathered_all[:, : micro_total * tokens]
    gathered = [gathered_all[:, k * tokens : (k + 1) * tokens] for k in range(2 * micro_total)]
    own_prep = half_weights(*own, row_blocks)
    own_all = half_values(own_prep, x_all, micro_total)
    own_first = half_branch(own_prep, own_all[0], gathered[micro_total])
    theirs, own_first = lax.optimization_barrier((theirs, own_first))
    their_prep = half_weights(*theirs, row_blocks)
    their_all = half_values(their_prep, x_all, micro_total)

    grads = []
    cot_full = gathered[micro_total]
    for micro_step in range(micro_total):
        own_values = own_all[micro_step]
        their_values = their_all[micro_step]
        if micro_step > 0:
            arrived, blocks = send_back_spread(grads[-1])
            cot_panel = jnp.where(last_section, seed_grad[0, micro_step], arrived)
            arrived_full = gather_bits(blocks, [2, 1], (3, 0))
            cot_full = jnp.where(last_section, gathered[micro_total + micro_step], arrived_full)
        else:
            cot_panel = seed_grad[0, 0]
        branch = own_first if micro_step == 0 else half_branch(own_prep, own_values, cot_full)
        branch = branch + half_branch(their_prep, their_values, cot_full)
        summed = reduce_scatter_tensor(branch)
        grads.append((cot_panel.astype(jnp.float32) + summed).astype(jnp.bfloat16))
    return jnp.stack(grads)[None]


def solution(mesh):
    return jax.shard_map(
        per_device,
        mesh=mesh,
        in_specs=(
            P("pipe", None, "tensor", None),
            P("pipe", None, "tensor", None),
            P("pipe", "tensor", None, None, None),
            P("pipe", "tensor", None, None, None),
            P("pipe", "tensor", None, None, None),
            P("pipe", "tensor", None, None),
            P("pipe", "tensor", None, None),
        ),
        out_specs=P("pipe", None, "tensor", None),
        check_vma=False,
    )
```

```python
import jax
import jax.numpy as jnp
from jax import lax
from jax.sharding import PartitionSpec as P

BLK = 64
RS_BITS = (0, 3, 1, 2)


def flip_pairs(axis, bit):
    return [(i, i ^ (1 << bit)) for i in range(lax.axis_size(axis))]


def from_behind(block, axis, distance):
    devices = range(lax.axis_size(axis))
    route = [(i - distance, i) for i in devices if i - distance in devices]
    return lax.ppermute(block, axis, route)


def reduce_scatter_tensor(value):
    t = lax.axis_index("tensor")
    n_bits = lax.axis_size("tensor").bit_length() - 1
    rows = value.shape[0] >> n_bits
    cur = value.reshape((2,) * n_bits + (rows, value.shape[1]))
    held = list(range(n_bits - 1, -1, -1))
    for bit in RS_BITS:
        axis = held.index(bit)
        mine = (t >> bit) & 1
        keep = lax.dynamic_index_in_dim(cur, mine, axis, keepdims=False)
        send = lax.dynamic_index_in_dim(cur, 1 - mine, axis, keepdims=False)
        cur = keep + lax.ppermute(send, "tensor", flip_pairs("tensor", bit))
        held.pop(axis)
    return cur


def gather_bits(cur, held, bits):
    t = lax.axis_index("tensor")
    held = list(held)
    for bit in bits:
        mine = (t >> bit) & 1
        recv = lax.ppermute(cur, "tensor", flip_pairs("tensor", bit))
        lo = jnp.where(mine == 0, cur, recv)
        hi = jnp.where(mine == 0, recv, cur)
        cur = jnp.stack([lo, hi], axis=0)
        held.insert(0, bit)
    order = sorted(range(len(held)), key=lambda i: -held[i])
    cur = jnp.transpose(cur, order + [len(held), len(held) + 1])
    rows = cur.shape[-2] << len(held)
    return cur.reshape(rows, cur.shape[-1])


def all_gather_tensor(panel):
    return gather_bits(panel, [], reversed(RS_BITS))


Y_FLIPS = (0, 2, 4, 6)


def send_back_spread(panel):
    n_pipe = lax.axis_size("pipe")
    n_tensor = lax.axis_size("tensor")
    recvs = []
    for flip in Y_FLIPS:
        route = [
            (src_p * n_tensor + src_t, (src_p - 2) * n_tensor + (src_t ^ flip))
            for src_p in range(2, n_pipe)
            for src_t in range(n_tensor)
        ]
        recvs.append(lax.ppermute(panel, ("pipe", "tensor"), route))
    t = lax.axis_index("tensor")
    blocks = jnp.stack(recvs).reshape((2, 2) + panel.shape)
    blocks = jnp.where(((t >> 2) & 1) == 1, blocks[::-1], blocks)
    blocks = jnp.where(((t >> 1) & 1) == 1, blocks[:, ::-1], blocks)
    return recvs[0], blocks


def half_weights(gate_blocks, up_blocks, down_blocks, gate_rows, down_rows, row_blocks):
    columns, slot_depth = gate_rows.shape
    tile_shape = (columns, slot_depth, BLK, BLK)
    pick = (gate_rows[:, :, None] == jnp.arange(row_blocks)[None, None, :]).astype(gate_blocks.dtype)
    spread = [
        jnp.einsum("crq,crf->cqf", pick, blocks, preferred_element_type=jnp.float32).astype(blocks.dtype)
        for blocks in (gate_blocks, up_blocks)
    ]
    dense = jnp.stack([part.reshape(columns, row_blocks, BLK, BLK) for part in spread], axis=3)
    dense = jnp.transpose(dense, (1, 2, 0, 3, 4)).reshape(row_blocks * BLK, columns * 2 * BLK)
    pick_d = (down_rows.reshape(-1)[:, None] == jnp.arange(row_blocks)[None, :]).astype(gate_blocks.dtype)
    return dense, down_blocks.reshape(tile_shape), pick_d


FEATURES = (((0,), (0,)), ((), ()))
HIDDEN = (((1,), (1,)), ((), ()))


def half_values(weights, x_all, micro_total):
    dense = weights[0]
    both = lax.dot_general(x_all, dense, FEATURES, preferred_element_type=jnp.float32)
    both = both.reshape(micro_total, -1, dense.shape[1] // (2 * BLK), 2 * BLK)
    return [both[k] for k in range(micro_total)]


def half_branch(weights, both, cot_full):
    dense, down_grid, pick_d = weights
    columns = down_grid.shape[0]
    tokens = cot_full.shape[1]
    row_blocks = pick_d.shape[1]
    cot_picked = jnp.dot(
        pick_d, cot_full.reshape(row_blocks, BLK * tokens), preferred_element_type=jnp.float32
    ).astype(cot_full.dtype).reshape(columns, -1, BLK, tokens)
    d_hidden = jnp.einsum("crjk,crkt->tcj", down_grid, cot_picked, preferred_element_type=jnp.float32)
    gate_value = both[:, :, :BLK]
    up_value = both[:, :, BLK:]
    sigmoid_gate = jax.nn.sigmoid(gate_value)
    d_gate = (
        d_hidden * up_value * sigmoid_gate * (1.0 + gate_value * (1.0 - sigmoid_gate))
    ).astype(jnp.bfloat16)
    d_up = (d_hidden * gate_value * sigmoid_gate).astype(jnp.bfloat16)
    d_both = jnp.concatenate([d_gate, d_up], axis=2).reshape(tokens, -1)
    return lax.dot_general(dense, d_both, HIDDEN, preferred_element_type=jnp.float32)


def per_device(x_saved, seed_grad, gate_blocks, up_blocks, down_blocks, gate_rows, down_rows):
    pipe_index = lax.axis_index("pipe")
    last_section = pipe_index // 2 == lax.axis_size("pipe") // 2 - 1
    own = tuple(a[0, 0] for a in (gate_blocks, up_blocks, down_blocks, gate_rows, down_rows))
    theirs = lax.ppermute(own, "pipe", flip_pairs("pipe", 0))
    micro_total = x_saved.shape[1]
    row_blocks = x_saved.shape[2] * lax.axis_size("tensor") // BLK

    tokens = x_saved.shape[3]
    first = jnp.concatenate([x_saved[0, k] for k in range(micro_total)] + [seed_grad[0, k] for k in range(micro_total)], axis=1)
    gathered_all = lax.all_gather(first, "tensor", axis=0, tiled=True)
    x_all = gathered_all[:, : micro_total * tokens]
    gathered = [gathered_all[:, k * tokens : (k + 1) * tokens] for k in range(2 * micro_total)]
    own_prep = half_weights(*own, row_blocks)
    their_prep = half_weights(*theirs, row_blocks)

    grads = []
    cot_full = gathered[micro_total]
    own_all = half_values(own_prep, x_all, micro_total)
    their_all = half_values(their_prep, x_all, micro_total)
    for micro_step in range(micro_total):
        own_values = own_all[micro_step]
        their_values = their_all[micro_step]
        if micro_step > 0:
            arrived, blocks = send_back_spread(grads[-1])
            cot_panel = jnp.where(last_section, seed_grad[0, micro_step], arrived)
            arrived_full = gather_bits(blocks, [2, 1], (3, 0))
            cot_full = jnp.where(last_section, gathered[micro_total + micro_step], arrived_full)
        else:
            cot_panel = seed_grad[0, 0]
        branch = half_branch(own_prep, own_values, cot_full)
        branch = branch + half_branch(their_prep, their_values, cot_full)
        summed = reduce_scatter_tensor(branch)
        grads.append((cot_panel.astype(jnp.float32) + summed).astype(jnp.bfloat16))
    return jnp.stack(grads)[None]


def solution(mesh):
    return jax.shard_map(
        per_device,
        mesh=mesh,
        in_specs=(
            P("pipe", None, "tensor", None),
            P("pipe", None, "tensor", None),
            P("pipe", "tensor", None, None, None),
            P("pipe", "tensor", None, None, None),
            P("pipe", "tensor", None, None, None),
            P("pipe", "tensor", None, None),
            P("pipe", "tensor", None, None),
        ),
        out_specs=P("pipe", None, "tensor", None),
        check_vma=False,
    )
```

```python
import jax
import jax.numpy as jnp
from jax import lax
from jax.sharding import PartitionSpec as P

BLK = 64
RS_BITS = (0, 3, 1, 2)


def flip_pairs(axis, bit):
    return [(i, i ^ (1 << bit)) for i in range(lax.axis_size(axis))]


def from_behind(block, axis, distance):
    devices = range(lax.axis_size(axis))
    route = [(i - distance, i) for i in devices if i - distance in devices]
    return lax.ppermute(block, axis, route)


def reduce_scatter_tensor(value):
    t = lax.axis_index("tensor")
    n_bits = lax.axis_size("tensor").bit_length() - 1
    rows = value.shape[0] >> n_bits
    cur = value.reshape((2,) * n_bits + (rows, value.shape[1]))
    held = list(range(n_bits - 1, -1, -1))
    for bit in RS_BITS[:2]:
        axis = held.index(bit)
        mine = (t >> bit) & 1
        keep = lax.dynamic_index_in_dim(cur, mine, axis, keepdims=False)
        send = lax.dynamic_index_in_dim(cur, 1 - mine, axis, keepdims=False)
        cur = keep + lax.ppermute(send, "tensor", flip_pairs("tensor", bit))
        held.pop(axis)
    assert held == [2, 1]
    hi, lo = (t >> 2) & 1, (t >> 1) & 1

    def block(flip):
        rows_hi = lax.dynamic_index_in_dim(cur, hi ^ ((flip >> 2) & 1), 0, keepdims=False)
        return lax.dynamic_index_in_dim(rows_hi, lo ^ ((flip >> 1) & 1), 0, keepdims=False)

    total = block(0)
    for flip in Y_FLIPS[1:]:
        total = total + lax.ppermute(block(flip), "tensor", [(i, i ^ flip) for i in range(lax.axis_size("tensor"))])
    return total


def gather_bits(cur, held, bits):
    t = lax.axis_index("tensor")
    held = list(held)
    for bit in bits:
        mine = (t >> bit) & 1
        recv = lax.ppermute(cur, "tensor", flip_pairs("tensor", bit))
        lo = jnp.where(mine == 0, cur, recv)
        hi = jnp.where(mine == 0, recv, cur)
        cur = jnp.stack([lo, hi], axis=0)
        held.insert(0, bit)
    order = sorted(range(len(held)), key=lambda i: -held[i])
    cur = jnp.transpose(cur, order + [len(held), len(held) + 1])
    rows = cur.shape[-2] << len(held)
    return cur.reshape(rows, cur.shape[-1])


def all_gather_tensor(panel):
    return gather_bits(panel, [], reversed(RS_BITS))


Y_FLIPS = (0, 2, 4, 6)


def send_back_spread(panel):
    n_pipe = lax.axis_size("pipe")
    n_tensor = lax.axis_size("tensor")
    recvs = []
    for flip in Y_FLIPS:
        route = [
            (src_p * n_tensor + src_t, (src_p - 2) * n_tensor + (src_t ^ flip))
            for src_p in range(2, n_pipe)
            for src_t in range(n_tensor)
        ]
        recvs.append(lax.ppermute(panel, ("pipe", "tensor"), route))
    t = lax.axis_index("tensor")
    blocks = jnp.stack(recvs).reshape((2, 2) + panel.shape)
    blocks = jnp.where(((t >> 2) & 1) == 1, blocks[::-1], blocks)
    blocks = jnp.where(((t >> 1) & 1) == 1, blocks[:, ::-1], blocks)
    return recvs[0], blocks


def half_weights(gate_blocks, up_blocks, down_blocks, gate_rows, down_rows, row_blocks):
    columns, slot_depth = gate_rows.shape
    tile_shape = (columns, slot_depth, BLK, BLK)
    paired = jnp.concatenate([gate_blocks.reshape(tile_shape), up_blocks.reshape(tile_shape)], axis=3)
    pick = (gate_rows[:, :, None] == jnp.arange(row_blocks)[None, None, :]).astype(paired.dtype)
    dense = jnp.einsum("crq,crkj->qkcj", pick, paired, preferred_element_type=jnp.float32)
    dense = dense.astype(paired.dtype).reshape(row_blocks * BLK, columns * 2 * BLK)
    pick_d = (down_rows.reshape(-1)[:, None] == jnp.arange(row_blocks)[None, :]).astype(paired.dtype)
    return dense, down_blocks.reshape(tile_shape), pick_d


FEATURES = (((0,), (0,)), ((), ()))
HIDDEN = (((1,), (1,)), ((), ()))


def half_values(weights, x_all, micro_total):
    dense = weights[0]
    both = lax.dot_general(x_all, dense, FEATURES, preferred_element_type=jnp.float32)
    both = both.reshape(micro_total, -1, dense.shape[1] // (2 * BLK), 2 * BLK)
    return [both[k] for k in range(micro_total)]


def half_branch(weights, both, cot_full):
    dense, down_grid, pick_d = weights
    columns = down_grid.shape[0]
    tokens = cot_full.shape[1]
    row_blocks = pick_d.shape[1]
    cot_picked = jnp.dot(
        pick_d, cot_full.reshape(row_blocks, BLK * tokens), preferred_element_type=jnp.float32
    ).astype(cot_full.dtype).reshape(columns, -1, BLK, tokens)
    d_hidden = jnp.einsum("crjk,crkt->tcj", down_grid, cot_picked, preferred_element_type=jnp.float32)
    gate_value = both[:, :, :BLK]
    up_value = both[:, :, BLK:]
    sigmoid_gate = jax.nn.sigmoid(gate_value)
    d_gate = (
        d_hidden * up_value * sigmoid_gate * (1.0 + gate_value * (1.0 - sigmoid_gate))
    ).astype(jnp.bfloat16)
    d_up = (d_hidden * gate_value * sigmoid_gate).astype(jnp.bfloat16)
    d_both = jnp.concatenate([d_gate, d_up], axis=2).reshape(tokens, -1)
    return lax.dot_general(dense, d_both, HIDDEN, preferred_element_type=jnp.float32)


def per_device(x_saved, seed_grad, gate_blocks, up_blocks, down_blocks, gate_rows, down_rows):
    pipe_index = lax.axis_index("pipe")
    last_section = pipe_index // 2 == lax.axis_size("pipe") // 2 - 1
    own = tuple(a[0, 0] for a in (gate_blocks, up_blocks, down_blocks, gate_rows, down_rows))
    theirs = lax.ppermute(own, "pipe", flip_pairs("pipe", 0))
    micro_total = x_saved.shape[1]
    row_blocks = x_saved.shape[2] * lax.axis_size("tensor") // BLK

    tokens = x_saved.shape[3]
    first = jnp.concatenate([x_saved[0, k] for k in range(micro_total)] + [seed_grad[0, k] for k in range(micro_total)], axis=1)
    gathered_all = lax.all_gather(first, "tensor", axis=0, tiled=True)
    x_all = gathered_all[:, : micro_total * tokens]
    gathered = [gathered_all[:, k * tokens : (k + 1) * tokens] for k in range(2 * micro_total)]
    own_prep = half_weights(*own, row_blocks)
    their_prep = half_weights(*theirs, row_blocks)

    grads = []
    cot_full = gathered[micro_total]
    own_all = half_values(own_prep, x_all, micro_total)
    their_all = half_values(their_prep, x_all, micro_total)
    for micro_step in range(micro_total):
        own_values = own_all[micro_step]
        their_values = their_all[micro_step]
        if micro_step > 0:
            arrived, blocks = send_back_spread(grads[-1])
            cot_panel = jnp.where(last_section, seed_grad[0, micro_step], arrived)
            arrived_full = gather_bits(blocks, [2, 1], (3, 0))
            cot_full = jnp.where(last_section, gathered[micro_total + micro_step], arrived_full)
        else:
            cot_panel = seed_grad[0, 0]
        branch = half_branch(own_prep, own_values, cot_full)
        branch = branch + half_branch(their_prep, their_values, cot_full)
        summed = reduce_scatter_tensor(branch)
        grads.append((cot_panel.astype(jnp.float32) + summed).astype(jnp.bfloat16))
    return jnp.stack(grads)[None]


def solution(mesh):
    return jax.shard_map(
        per_device,
        mesh=mesh,
        in_specs=(
            P("pipe", None, "tensor", None),
            P("pipe", None, "tensor", None),
            P("pipe", "tensor", None, None, None),
            P("pipe", "tensor", None, None, None),
            P("pipe", "tensor", None, None, None),
            P("pipe", "tensor", None, None),
            P("pipe", "tensor", None, None),
        ),
        out_specs=P("pipe", None, "tensor", None),
        check_vma=False,
    )
```

```python
import jax
import jax.numpy as jnp
from jax import lax
from jax.sharding import PartitionSpec as P

BLK = 64
RS_BITS = (0, 3, 1, 2)


def flip_pairs(axis, bit):
    return [(i, i ^ (1 << bit)) for i in range(lax.axis_size(axis))]


def from_behind(block, axis, distance):
    devices = range(lax.axis_size(axis))
    route = [(i - distance, i) for i in devices if i - distance in devices]
    return lax.ppermute(block, axis, route)


def reduce_scatter_tensor(value):
    t = lax.axis_index("tensor")
    n_bits = lax.axis_size("tensor").bit_length() - 1
    rows = value.shape[0] >> n_bits
    cur = value.reshape((2,) * n_bits + (rows, value.shape[1]))
    held = list(range(n_bits - 1, -1, -1))
    for bit in RS_BITS[:2]:
        axis = held.index(bit)
        mine = (t >> bit) & 1
        keep = lax.dynamic_index_in_dim(cur, mine, axis, keepdims=False)
        send = lax.dynamic_index_in_dim(cur, 1 - mine, axis, keepdims=False)
        cur = keep + lax.ppermute(send, "tensor", flip_pairs("tensor", bit))
        held.pop(axis)
    assert held == [2, 1]
    hi, lo = (t >> 2) & 1, (t >> 1) & 1

    def block(flip):
        rows_hi = lax.dynamic_index_in_dim(cur, hi ^ ((flip >> 2) & 1), 0, keepdims=False)
        return lax.dynamic_index_in_dim(rows_hi, lo ^ ((flip >> 1) & 1), 0, keepdims=False)

    total = block(0)
    for flip in Y_FLIPS[1:]:
        total = total + lax.ppermute(block(flip), "tensor", [(i, i ^ flip) for i in range(lax.axis_size("tensor"))])
    return total


def gather_bits(cur, held, bits):
    t = lax.axis_index("tensor")
    held = list(held)
    for bit in bits:
        mine = (t >> bit) & 1
        recv = lax.ppermute(cur, "tensor", flip_pairs("tensor", bit))
        lo = jnp.where(mine == 0, cur, recv)
        hi = jnp.where(mine == 0, recv, cur)
        cur = jnp.stack([lo, hi], axis=0)
        held.insert(0, bit)
    order = sorted(range(len(held)), key=lambda i: -held[i])
    cur = jnp.transpose(cur, order + [len(held), len(held) + 1])
    rows = cur.shape[-2] << len(held)
    return cur.reshape(rows, cur.shape[-1])


def all_gather_tensor(panel):
    return gather_bits(panel, [], reversed(RS_BITS))


Y_FLIPS = (0, 2, 4, 6)


SEND_FLIPS = tuple(range(0, 16, 2))


def send_back_spread(panel):
    n_pipe = lax.axis_size("pipe")
    n_tensor = lax.axis_size("tensor")
    recvs = []
    for flip in SEND_FLIPS:
        route = [
            (src_p * n_tensor + src_t, (src_p - 2) * n_tensor + (src_t ^ flip))
            for src_p in range(2, n_pipe)
            for src_t in range(n_tensor)
        ]
        recvs.append(lax.ppermute(panel, ("pipe", "tensor"), route))
    t = lax.axis_index("tensor")
    blocks = jnp.stack(recvs).reshape((2, 2, 2) + panel.shape)
    blocks = jnp.where(((t >> 3) & 1) == 1, blocks[::-1], blocks)
    blocks = jnp.where(((t >> 2) & 1) == 1, blocks[:, ::-1], blocks)
    blocks = jnp.where(((t >> 1) & 1) == 1, blocks[:, :, ::-1], blocks)
    return recvs[0], blocks


def half_weights(gate_blocks, up_blocks, down_blocks, gate_rows, down_rows, row_blocks):
    columns, slot_depth = gate_rows.shape
    tile_shape = (columns, slot_depth, BLK, BLK)
    paired = jnp.concatenate([gate_blocks.reshape(tile_shape), up_blocks.reshape(tile_shape)], axis=3)
    pick = (gate_rows[:, :, None] == jnp.arange(row_blocks)[None, None, :]).astype(paired.dtype)
    dense = jnp.einsum("crq,crkj->qkcj", pick, paired, preferred_element_type=jnp.float32)
    dense = dense.astype(paired.dtype).reshape(row_blocks * BLK, columns * 2 * BLK)
    pick_d = (down_rows.reshape(-1)[:, None] == jnp.arange(row_blocks)[None, :]).astype(paired.dtype)
    return dense, down_blocks.reshape(tile_shape), pick_d


FEATURES = (((0,), (0,)), ((), ()))
HIDDEN = (((1,), (1,)), ((), ()))


def half_values(weights, x_all, micro_total):
    dense = weights[0]
    both = lax.dot_general(x_all, dense, FEATURES, preferred_element_type=jnp.float32)
    both = both.reshape(micro_total, -1, dense.shape[1] // (2 * BLK), 2 * BLK)
    return [both[k] for k in range(micro_total)]


def half_branch(weights, both, cot_full):
    dense, down_grid, pick_d = weights
    columns = down_grid.shape[0]
    tokens = cot_full.shape[1]
    row_blocks = pick_d.shape[1]
    cot_picked = jnp.dot(
        pick_d, cot_full.reshape(row_blocks, BLK * tokens), preferred_element_type=jnp.float32
    ).astype(cot_full.dtype).reshape(columns, -1, BLK, tokens)
    d_hidden = jnp.einsum("crjk,crkt->tcj", down_grid, cot_picked, preferred_element_type=jnp.float32)
    gate_value = both[:, :, :BLK]
    up_value = both[:, :, BLK:]
    sigmoid_gate = jax.nn.sigmoid(gate_value)
    d_gate = (
        d_hidden * up_value * sigmoid_gate * (1.0 + gate_value * (1.0 - sigmoid_gate))
    ).astype(jnp.bfloat16)
    d_up = (d_hidden * gate_value * sigmoid_gate).astype(jnp.bfloat16)
    d_both = jnp.concatenate([d_gate, d_up], axis=2).reshape(tokens, -1)
    return lax.dot_general(dense, d_both, HIDDEN, preferred_element_type=jnp.float32)


def per_device(x_saved, seed_grad, gate_blocks, up_blocks, down_blocks, gate_rows, down_rows):
    pipe_index = lax.axis_index("pipe")
    last_section = pipe_index // 2 == lax.axis_size("pipe") // 2 - 1
    own = tuple(a[0, 0] for a in (gate_blocks, up_blocks, down_blocks, gate_rows, down_rows))
    theirs = lax.ppermute(own, "pipe", flip_pairs("pipe", 0))
    micro_total = x_saved.shape[1]
    row_blocks = x_saved.shape[2] * lax.axis_size("tensor") // BLK

    tokens = x_saved.shape[3]
    first = jnp.concatenate([x_saved[0, k] for k in range(micro_total)] + [seed_grad[0, k] for k in range(micro_total)], axis=1)
    gathered_all = lax.all_gather(first, "tensor", axis=0, tiled=True)
    x_all = gathered_all[:, : micro_total * tokens]
    gathered = [gathered_all[:, k * tokens : (k + 1) * tokens] for k in range(2 * micro_total)]
    own_prep = half_weights(*own, row_blocks)
    their_prep = half_weights(*theirs, row_blocks)

    grads = []
    cot_full = gathered[micro_total]
    own_all = half_values(own_prep, x_all, micro_total)
    their_all = half_values(their_prep, x_all, micro_total)
    for micro_step in range(micro_total):
        own_values = own_all[micro_step]
        their_values = their_all[micro_step]
        if micro_step > 0:
            arrived, blocks = send_back_spread(grads[-1])
            cot_panel = jnp.where(last_section, seed_grad[0, micro_step], arrived)
            arrived_full = gather_bits(blocks, [3, 2, 1], (0,))
            cot_full = jnp.where(last_section, gathered[micro_total + micro_step], arrived_full)
        else:
            cot_panel = seed_grad[0, 0]
        branch = half_branch(own_prep, own_values, cot_full)
        branch = branch + half_branch(their_prep, their_values, cot_full)
        summed = reduce_scatter_tensor(branch)
        grads.append((cot_panel.astype(jnp.float32) + summed).astype(jnp.bfloat16))
    return jnp.stack(grads)[None]


def solution(mesh):
    return jax.shard_map(
        per_device,
        mesh=mesh,
        in_specs=(
            P("pipe", None, "tensor", None),
            P("pipe", None, "tensor", None),
            P("pipe", "tensor", None, None, None),
            P("pipe", "tensor", None, None, None),
            P("pipe", "tensor", None, None, None),
            P("pipe", "tensor", None, None),
            P("pipe", "tensor", None, None),
        ),
        out_specs=P("pipe", None, "tensor", None),
        check_vma=False,
    )
```
